128 devices in a mesh: grp: 8 (over y, core), shard: 16 (over z, x).
Axes of the slice: x: 4, y: 4, z: 4, core: 2. Of those that a mesh axis runs over, the one named last changes fastest.
Arguments:
- tokens: bfloat16 [65536, 2560], P(('grp', 'shard')), may hold values from -6 to 6
- gain: float32 [2560], replicated, may hold values from 0.25 to 1.75
- w_qkv: bfloat16 [2560, 3072], P(None, 'shard'), may hold values from -1 to 1
- prefix_kv: bfloat16 [8, 2048, 512], P('grp', 'shard'), may hold values from -6 to 6
- prefix_owner: int32 [8], P('grp'), may hold values from 0 to 7, as said below
- suffix_len: int32 [8, 16], P('grp', 'shard'), may hold values from 1 to 512, 5120 in all within a row
- slots: int32 [8, 8192], P('grp', 'shard'), may hold values from 0 to 8191, as said below
Outputs:
- attended: bfloat16 [65536, 2560], P(('grp', 'shard'))
The draws below stay inside these ranges and needn't reach their ends.
Inputs may be any that keep to these rules, and one draw needn't show every extreme that they name: In each group the slots are a permutation of 0 to 8191; in each aligned run of 512 entries the k-th block of 32 entries holds slots k * 512 to (k + 1) * 512 - 1. `suffix_len`: each group's lengths sum to 5120 and one of them equals 512. `prefix_owner`: each entry names one of the 8 caches; several groups may name the same one.
All inputs are finite; a program needn't handle non-finite values.
Results may differ from the reference program's by a relative error of at most 0.0069.
Values may be sent and summed in bfloat16 or wider, within the bound.
No kernel may reach another device: no remote copies, remote signals or barrier semaphores. Data moves between devices by JAX's collectives and lax.ppermute only.
A program may use at most 128 MiB of HBM per device.

```python
import math
import jax
import jax.numpy as jnp
import numpy as np
from jax import lax

D = 2560
H = 10
HD = 256
WINDOW = 2048
SUF = 512
PRE = 2048
GROUPS = 8
TOK_DEV = 512
REQ = 16
TOKG = 8192
HQ = 2560
QKV = 3072


def draw_slots(key, part):
    shard_count = TOKG // TOK_DEV
    block = TOK_DEV // shard_count
    keys = jax.random.split(key, GROUPS * shard_count)

    def shuffle(single):
        return jax.random.permutation(single, TOK_DEV)
    orders = jax.vmap(shuffle)(keys).astype(jnp.int32)
    orders = orders.reshape(GROUPS, shard_count, shard_count, block)
    offsets = jnp.arange(shard_count, dtype=jnp.int32) * TOK_DEV
    orders = orders + offsets[None, :, None, None]
    return orders.transpose(0, 2, 1, 3).reshape(GROUPS, TOKG).astype(jnp.int32)


def draw_prefix_owner(key, part):
    own_key = jax.random.fold_in(key, 53)
    pick_key, perm_key = jax.random.split(own_key)
    rest = GROUPS - 2
    choices_at = jnp.array([1, GROUPS // 2, 0, -1], dtype=jnp.int32)
    picks = jax.random.randint(pick_key, (rest,), 0, 4).astype(jnp.int32)
    chosen = jnp.sum(jnp.where(picks[:, None] == jnp.arange(4, dtype=jnp.int32)[None, :], choices_at[None, :], 0), axis=1).astype(jnp.int32)
    offsets = jnp.concatenate([jnp.array([-1, -1], dtype=jnp.int32), chosen])
    groups_at = jnp.arange(GROUPS, dtype=jnp.int32)
    owners = ((groups_at + offsets + GROUPS) % GROUPS).astype(jnp.int32)
    placement = jax.random.permutation(perm_key, GROUPS).astype(jnp.int32)
    return owners[placement].astype(jnp.int32)


def draw_tokens(key, part):
    own_key = jax.random.fold_in(key, 11)
    noise_key = jax.random.fold_in(own_key, 0)
    extent = (GROUPS * TOKG, D)
    drawn_rows = jax.random.normal(noise_key, extent, jnp.float32)
    return jnp.clip(drawn_rows, -6.0, 6.0).astype(jnp.bfloat16)


def draw_w_qkv(key, part):
    own_key = jax.random.fold_in(key, 23)
    extent = (D, QKV)
    spread = D ** (-0.5)
    sample = jnp.clip(jax.random.normal(own_key, extent, jnp.float32), -6.0, 6.0) * spread
    return sample.astype(jnp.bfloat16)


def draw_prefix_kv(key, part):
    own_key = jax.random.fold_in(key, 37)
    extent = (GROUPS, PRE, 2 * HD)
    pool_rows = jnp.clip(jax.random.normal(own_key, extent, jnp.float32), -6.0, 6.0)
    return pool_rows.astype(jnp.bfloat16)


def split_up(number_of, total, most, lean):
    weights = [(1 << 20) // math.isqrt(standing ** lean) + 1 for standing in range(2, number_of + 1)]
    surplus, given = total - most - (number_of - 1), [1] * (number_of - 1)
    while surplus > 0:
        candidates = [i for i in range(number_of - 1) if given[i] < most]
        mass, remaining = sum([weights[i] for i in candidates]), surplus
        for i in candidates:
            extra = min(most - given[i], max(1, remaining * weights[i] // mass), surplus)
            given[i] = given[i] + extra
            surplus = surplus - extra
    return np.array([most] + given)


def ragged_sizes(stream_key, amount, total, bound, skew):
    if amount == 2:
        one = jax.random.randint(stream_key, (), max(1, total - bound), min(bound, total - 1) + 1)
        return jnp.stack([one, total - one])
    sizes = jnp.asarray(split_up(amount, total, bound, skew), jnp.int32)
    couples = (amount - 1) // 2
    source_of, receiver = sizes[1:1 + 2 * couples:2], sizes[2:2 + 2 * couples:2]
    slack = jnp.minimum(source_of - 1, bound - receiver)
    moved = jax.random.randint(jax.random.fold_in(stream_key, 1), (couples,), 0, 1 << 20) % (slack + 1)
    sizes = sizes.at[1:1 + 2 * couples:2].set(source_of - moved).at[2:2 + 2 * couples:2].set(receiver + moved)
    return sizes[jax.random.permutation(jax.random.fold_in(stream_key, 2), amount)]


def setup_inputs(seed: int = 0) -> dict:
    seeds = jax.random.split(jax.random.key(seed), 8)
    tokens = draw_tokens(jax.random.fold_in(seeds[7], 71), 0)
    gain = jnp.clip(1.0 + 0.15 * jax.random.normal(seeds[1], (D,), jnp.float32), 0.25, 1.75)
    w_qkv = draw_w_qkv(jax.random.fold_in(seeds[7], 71), 0)
    prefix_kv = draw_prefix_kv(jax.random.fold_in(seeds[7], 71), 0)
    prefix_owner = draw_prefix_owner(jax.random.fold_in(seeds[7], 71), 0)
    suffix_len = jax.vmap(lambda own: ragged_sizes(own, REQ, 5 * REQ * SUF // 8, SUF, 2))(jax.random.split(seeds[5], GROUPS)).reshape((GROUPS, REQ)).astype(jnp.int32)
    slots = draw_slots(jax.random.fold_in(seeds[7], 71), 0)
    return {"tokens": tokens, "gain": gain, "w_qkv": w_qkv, "prefix_kv": prefix_kv, "prefix_owner": prefix_owner, "suffix_len": suffix_len, "slots": slots}


def normalize(rows, gain):
    rows32 = rows.astype(jnp.float32)
    factor = lax.rsqrt(lax.optimization_barrier(jnp.mean(rows32 * rows32, axis=-1, keepdims=True)) + 1e-06)
    return (rows32 * factor * gain.astype(jnp.float32)).astype(jnp.bfloat16)

def attend_request(queries, suffix_kv, prefix, length):
    keys = jnp.concatenate([prefix[:, :HD], suffix_kv[:, :HD]], axis=0)
    values = jnp.concatenate([prefix[:, HD:], suffix_kv[:, HD:]], axis=0)
    span = keys.shape[0]
    prefix_len = prefix.shape[0]
    count = queries.shape[0]
    query_pos = jnp.arange(count, dtype=jnp.int32)[:, None]
    key_pos = jnp.arange(span, dtype=jnp.int32)[None, :]
    visible = (key_pos > prefix_len + query_pos - WINDOW) & (key_pos <= prefix_len + query_pos) & (key_pos < prefix_len + length)
    heads = queries.reshape(count, H, HD).transpose(1, 0, 2)

    def one_head(head_q):
        scores = jnp.dot(head_q, keys.T, preferred_element_type=jnp.float32) * HD ** (-0.5)
        scores = jnp.where(visible, scores, -1e+30)
        top = lax.optimization_barrier(jnp.max(scores, axis=-1, keepdims=True))
        expd = jnp.exp(scores - top)
        weights = (expd / lax.optimization_barrier(jnp.sum(expd, axis=-1, keepdims=True))).astype(jnp.bfloat16)
        return jnp.dot(weights, values, preferred_element_type=jnp.float32)
    result = lax.map(one_head, heads).transpose(1, 0, 2).reshape(count, H * HD)
    return jnp.where(query_pos < length, result, 0.0).astype(jnp.bfloat16)

def reference(tokens, gain, w_qkv, prefix_kv, prefix_owner, suffix_len, slots):
    grouped = tokens.reshape(GROUPS, TOKG, D)

    def one_group(items):
        rows, order, owner, lengths = items
        normed = normalize(rows, gain)
        qkv = jnp.dot(normed, w_qkv, preferred_element_type=jnp.float32).astype(jnp.bfloat16)
        placed = jnp.zeros_like(qkv).at[order].set(qkv).reshape(REQ, SUF, QKV)
        prefix = lax.dynamic_index_in_dim(prefix_kv, owner, 0, keepdims=False)

        def one_request(pair):
            block, length = pair
            return attend_request(block[:, :HQ], block[:, HQ:], prefix, length)
        return lax.map(one_request, (placed, lengths)).reshape(TOKG, HQ)
    result = lax.map(one_group, (grouped, slots, prefix_owner, suffix_len))
    return result.reshape(GROUPS * TOKG, HQ)
```

```python
import jax
import jax.numpy as jnp
from jax import lax
from jax.sharding import PartitionSpec as P

H = 10
HD = 256
WINDOW = 2048
SUF = 512
HQ = 2560


def normalize(rows, gain):
    rows32 = rows.astype(jnp.float32)
    factor = lax.rsqrt(jnp.mean(rows32 * rows32, axis=-1, keepdims=True) + 1e-06)
    return (rows32 * factor * gain).astype(jnp.bfloat16)


def attend_request(queries, suffix_kv, prefix, length):
    keys = jnp.concatenate([prefix[:, :HD], suffix_kv[:, :HD]], axis=0)
    values = jnp.concatenate([prefix[:, HD:], suffix_kv[:, HD:]], axis=0)
    span = keys.shape[0]
    prefix_len = prefix.shape[0]
    count = queries.shape[0]
    query_pos = jnp.arange(count, dtype=jnp.int32)[:, None]
    key_pos = jnp.arange(span, dtype=jnp.int32)[None, :]
    visible = (
        (key_pos > prefix_len + query_pos - WINDOW)
        & (key_pos <= prefix_len + query_pos)
        & (key_pos < prefix_len + length)
    )
    heads = queries.reshape(count, H, HD).transpose(1, 0, 2)

    def one_head(head_q):
        scores = jnp.dot(head_q, keys.T, preferred_element_type=jnp.float32) * HD ** (-0.5)
        scores = jnp.where(visible, scores, -1e30)
        top = jnp.max(scores, axis=-1, keepdims=True)
        expd = jnp.exp(scores - top)
        weights = (expd / jnp.sum(expd, axis=-1, keepdims=True)).astype(jnp.bfloat16)
        return jnp.dot(weights, values, preferred_element_type=jnp.float32)

    result = lax.map(one_head, heads).transpose(1, 0, 2).reshape(count, H * HD)
    return jnp.where(query_pos < length, result, 0.0).astype(jnp.bfloat16)


def gather_by_a2a(piece, axis_name, count):
    spread = jnp.broadcast_to(piece[None], (count,) + piece.shape)
    return lax.all_to_all(spread, axis_name, 0, 0, tiled=True)


def shards(tokens, gain, w_qkv, prefix_kv, prefix_owner, suffix_len, slots):
    tok_dev = tokens.shape[0]
    n_grp = lax.axis_size("grp")
    n_shard = lax.axis_size("shard")
    grp = lax.axis_index("grp")
    core = grp % 2
    pairs = [(g, g ^ 1) for g in range(n_grp)]

    normed = normalize(tokens, gain)
    partner_rows = lax.ppermute(normed, "grp", pairs)

    cols = w_qkv.shape[1]
    half = cols // 2
    w_mine = lax.dynamic_slice_in_dim(w_qkv, core * half, half, axis=1)
    w_gathered = lax.all_gather(w_mine, "shard", axis=1, tiled=True)
    both = jnp.concatenate([normed, partner_rows], axis=0)
    out = jnp.dot(both, w_gathered, preferred_element_type=jnp.float32).astype(jnp.bfloat16)
    out_mine = out[:tok_dev]
    out_back = lax.ppermute(out[tok_dev:], "grp", pairs)
    is0 = core == 0
    half0 = jnp.where(is0, out_mine, out_back).reshape(tok_dev, n_shard, 1, half)
    half1 = jnp.where(is0, out_back, out_mine).reshape(tok_dev, n_shard, 1, half)
    projected = jnp.concatenate([half0, half1], axis=2).reshape(tok_dev, n_shard * cols)

    order = slots.reshape(tok_dev)
    arrived, order = (
        lax.all_to_all(projected, "shard", split_axis=0, concat_axis=0, tiled=True),
        lax.all_to_all(order, "shard", split_axis=0, concat_axis=0, tiled=True),
    )
    first_slot = lax.axis_index("shard") * tok_dev
    pos = order - first_slot
    onehot = (jnp.arange(tok_dev, dtype=jnp.int32)[:, None] == pos[None, :]).astype(jnp.bfloat16)
    placed = jnp.dot(onehot, arrived, preferred_element_type=jnp.float32).astype(jnp.bfloat16)

    owner = prefix_owner[0]
    sliced = gather_by_a2a(prefix_kv[0], "grp", n_grp)
    chosen = lax.dynamic_index_in_dim(sliced, owner, 0, keepdims=False)
    prefix = gather_by_a2a(chosen, "shard", n_shard).reshape(-1, chosen.shape[-1])

    lengths = suffix_len.reshape(-1)
    results = attend_request(placed[:, :HQ], placed[:, HQ:], prefix, lengths[0])
    return results


def solution(mesh):
    return jax.shard_map(
        shards,
        mesh=mesh,
        in_specs=(
            P(("grp", "shard"), None),
            P(),
            P(None, "shard"),
            P("grp", "shard", None),
            P("grp"),
            P("grp", "shard"),
            P("grp", "shard"),
        ),
        out_specs=P(("grp", "shard"), None),
        check_vma=False,
    )
```

```python
import jax
import jax.numpy as jnp
from jax import lax
from jax.experimental import pallas as pl
from jax.experimental.pallas import tpu as pltpu
from jax.sharding import PartitionSpec as P

H = 10
HD = 256
WINDOW = 2048
SUF = 512
HQ = 2560
TQ = 128


def normalize(rows, gain):
    rows32 = rows.astype(jnp.float32)
    factor = lax.rsqrt(jnp.mean(rows32 * rows32, axis=-1, keepdims=True) + 1e-06)
    return (rows32 * factor * gain).astype(jnp.bfloat16)


def _attn_kernel(len_ref, q_ref, pk_ref, pv_ref, sk_ref, sv_ref, o_ref):
    n = len_ref[0]
    pre = pk_ref.shape[0]
    count = q_ref.shape[0]
    scale = HD ** (-0.5)
    nt = (((1,), (1,)), ((), ()))
    for i in range(count // TQ):
        r0 = i * TQ
        q = q_ref[r0:r0 + TQ, :]
        qpos = r0 + lax.broadcasted_iota(jnp.int32, (TQ, 1), 0)
        sp = lax.dot_general(q, pk_ref[r0:, :], nt, preferred_element_type=jnp.float32) * scale
        ppos = r0 + lax.broadcasted_iota(jnp.int32, (1, pre - r0), 1)
        vis_p = (ppos > pre + qpos - WINDOW) & (ppos <= pre + qpos) & (ppos < pre + n)
        sp = jnp.where(vis_p, sp, -1e30)
        ns = r0 + TQ
        ss = lax.dot_general(q, sk_ref[:ns, :], nt, preferred_element_type=jnp.float32) * scale
        spos = pre + lax.broadcasted_iota(jnp.int32, (1, ns), 1)
        vis_s = (spos > pre + qpos - WINDOW) & (spos <= pre + qpos) & (spos < pre + n)
        ss = jnp.where(vis_s, ss, -1e30)
        top = jnp.maximum(jnp.max(sp, axis=-1, keepdims=True), jnp.max(ss, axis=-1, keepdims=True))
        ep = jnp.exp(sp - top)
        es = jnp.exp(ss - top)
        total = jnp.sum(ep, axis=-1, keepdims=True) + jnp.sum(es, axis=-1, keepdims=True)
        inv = 1.0 / total
        wp = (ep * inv).astype(jnp.bfloat16)
        ws = (es * inv).astype(jnp.bfloat16)
        acc = jnp.dot(wp, pv_ref[r0:, :], preferred_element_type=jnp.float32)
        acc = acc + jnp.dot(ws, sv_ref[:ns, :], preferred_element_type=jnp.float32)
        o_ref[r0:r0 + TQ, :] = jnp.where(qpos < n, acc, 0.0).astype(o_ref.dtype)


def attend(qkv, prefix, length):
    count = qkv.shape[0]
    pre = prefix.shape[0]
    grid_spec = pltpu.PrefetchScalarGridSpec(
        num_scalar_prefetch=1,
        grid=(H,),
        in_specs=[
            pl.BlockSpec((count, HD), lambda h, n: (0, h)),
            pl.BlockSpec((pre, HD), lambda h, n: (0, 0)),
            pl.BlockSpec((pre, HD), lambda h, n: (0, 1)),
            pl.BlockSpec((count, HD), lambda h, n: (0, H)),
            pl.BlockSpec((count, HD), lambda h, n: (0, H + 1)),
        ],
        out_specs=pl.BlockSpec((count, HD), lambda h, n: (0, h)),
    )
    flops = 4 * H * count * (pre + count) * HD
    return pl.pallas_call(
        _attn_kernel,
        out_shape=jax.ShapeDtypeStruct((count, H * HD), jnp.bfloat16),
        grid_spec=grid_spec,
        compiler_params=pltpu.CompilerParams(vmem_limit_bytes=48 * 1024 * 1024),
        cost_estimate=pl.CostEstimate(
            flops=flops,
            transcendentals=H * count * (pre + count),
            bytes_accessed=2 * (count * qkv.shape[1] + pre * prefix.shape[1] + count * H * HD),
        ),
    )(length.reshape(1).astype(jnp.int32), qkv, prefix, prefix, qkv, qkv)


def gather_by_a2a(piece, axis_name, count):
    spread = jnp.broadcast_to(piece[None], (count,) + piece.shape)
    return lax.all_to_all(spread, axis_name, 0, 0, tiled=True)


def shards(tokens, gain, w_qkv, prefix_kv, prefix_owner, suffix_len, slots):
    tok_dev = tokens.shape[0]
    n_grp = lax.axis_size("grp")
    n_shard = lax.axis_size("shard")
    core = lax.axis_index("grp") % 2
    pairs = [(g, g ^ 1) for g in range(n_grp)]

    owner = prefix_owner[0]
    sliced = gather_by_a2a(prefix_kv[0], "grp", n_grp)
    chosen = lax.dynamic_index_in_dim(sliced, owner, 0, keepdims=False)
    prefix = gather_by_a2a(chosen, "shard", n_shard).reshape(-1, chosen.shape[-1])

    order = slots.reshape(tok_dev)
    arrived = lax.all_to_all(tokens, "shard", 0, 0, tiled=True)
    order = lax.all_to_all(order, "shard", 0, 0, tiled=True)
    pos = order - lax.axis_index("shard") * tok_dev
    onehot = (jnp.arange(tok_dev, dtype=jnp.int32)[:, None] == pos[None, :]).astype(jnp.bfloat16)
    placed = jnp.dot(onehot, arrived, preferred_element_type=jnp.float32).astype(jnp.bfloat16)
    normed = normalize(placed, gain)

    d = w_qkv.shape[0]
    kh = d // 2
    w_mine = lax.dynamic_slice_in_dim(w_qkv, core * kh, kh, axis=0)
    w_rows = lax.all_gather(w_mine, "shard", axis=1, tiled=True)
    w_other = lax.ppermute(w_rows, "grp", pairs)
    n_mine = lax.dynamic_slice_in_dim(normed, core * kh, kh, axis=1)
    n_other = lax.dynamic_slice_in_dim(normed, (1 - core) * kh, kh, axis=1)
    acc = jnp.dot(n_mine, w_rows, preferred_element_type=jnp.float32)
    acc = acc + jnp.dot(n_other, w_other, preferred_element_type=jnp.float32)
    qkv = acc.astype(jnp.bfloat16)

    lengths = suffix_len.reshape(-1)
    return attend(qkv, prefix, lengths[0])


def solution(mesh):
    return jax.shard_map(
        shards,
        mesh=mesh,
        in_specs=(
            P(("grp", "shard"), None),
            P(),
            P(None, "shard"),
            P("grp", "shard", None),
            P("grp"),
            P("grp", "shard"),
            P("grp", "shard"),
        ),
        out_specs=P(("grp", "shard"), None),
        check_vma=False,
    )
```

```python
import jax
import jax.numpy as jnp
from jax import lax
from jax.experimental import pallas as pl
from jax.experimental.pallas import tpu as pltpu
from jax.sharding import PartitionSpec as P


H = 10
HD = 256
WINDOW = 2048
TQ = 128


def normalize(rows, gain):
    rows32 = rows.astype(jnp.float32)
    factor = lax.rsqrt(jnp.mean(rows32 * rows32, axis=-1, keepdims=True) + 1e-06)
    return (rows32 * factor * gain).astype(jnp.bfloat16)


def _attn_kernel(len_ref, q_ref, pk_ref, pv_ref, sk_ref, sv_ref, o_ref):
    n = len_ref[0]
    pre = pk_ref.shape[0]
    count = q_ref.shape[0]
    scale = HD ** (-0.5)
    nt = (((1,), (1,)), ((), ()))
    for i in range(count // TQ):
        r0 = i * TQ
        q = q_ref[r0:r0 + TQ, :]
        qpos = r0 + lax.broadcasted_iota(jnp.int32, (TQ, 1), 0)
        sp = lax.dot_general(q, pk_ref[r0:, :], nt, preferred_element_type=jnp.float32) * scale
        ppos = r0 + lax.broadcasted_iota(jnp.int32, (1, pre - r0), 1)
        vis_p = (ppos > pre + qpos - WINDOW) & (ppos <= pre + qpos) & (ppos < pre + n)
        sp = jnp.where(vis_p, sp, -1e30)
        ns = r0 + TQ
        ss = lax.dot_general(q, sk_ref[:ns, :], nt, preferred_element_type=jnp.float32) * scale
        spos = pre + lax.broadcasted_iota(jnp.int32, (1, ns), 1)
        vis_s = (spos > pre + qpos - WINDOW) & (spos <= pre + qpos) & (spos < pre + n)
        ss = jnp.where(vis_s, ss, -1e30)
        top = jnp.maximum(jnp.max(sp, axis=-1, keepdims=True), jnp.max(ss, axis=-1, keepdims=True))
        ep = jnp.exp(sp - top)
        es = jnp.exp(ss - top)
        total = jnp.sum(ep, axis=-1, keepdims=True) + jnp.sum(es, axis=-1, keepdims=True)
        inv = 1.0 / total
        wp = (ep * inv).astype(jnp.bfloat16)
        ws = (es * inv).astype(jnp.bfloat16)
        acc = jnp.dot(wp, pv_ref[r0:, :], preferred_element_type=jnp.float32)
        acc = acc + jnp.dot(ws, sv_ref[:ns, :], preferred_element_type=jnp.float32)
        o_ref[r0:r0 + TQ, :] = jnp.where(qpos < n, acc, 0.0).astype(o_ref.dtype)


def attend(qkv, prefix, length):
    count = qkv.shape[0]
    pre = prefix.shape[0]
    grid_spec = pltpu.PrefetchScalarGridSpec(
        num_scalar_prefetch=1,
        grid=(H,),
        in_specs=[
            pl.BlockSpec((count, HD), lambda h, n: (0, h)),
            pl.BlockSpec((pre, HD), lambda h, n: (0, 0)),
            pl.BlockSpec((pre, HD), lambda h, n: (0, 1)),
            pl.BlockSpec((count, HD), lambda h, n: (0, H)),
            pl.BlockSpec((count, HD), lambda h, n: (0, H + 1)),
        ],
        out_specs=pl.BlockSpec((count, HD), lambda h, n: (0, h)),
    )
    flops = 4 * H * count * (pre + count) * HD
    return pl.pallas_call(
        _attn_kernel,
        out_shape=jax.ShapeDtypeStruct((count, H * HD), jnp.bfloat16),
        grid_spec=grid_spec,
        compiler_params=pltpu.CompilerParams(vmem_limit_bytes=48 * 1024 * 1024),
        cost_estimate=pl.CostEstimate(
            flops=flops,
            transcendentals=H * count * (pre + count),
            bytes_accessed=2 * (count * qkv.shape[1] + pre * prefix.shape[1] + count * H * HD),
        ),
    )(length.reshape(1).astype(jnp.int32), qkv, prefix, prefix, qkv, qkv)


def gather_by_a2a(piece, axis_name, count):
    spread = jnp.broadcast_to(piece[None], (count,) + piece.shape)
    return lax.all_to_all(spread, axis_name, 0, 0, tiled=True)


def shards(tokens, gain, w_qkv, prefix_kv, prefix_owner, suffix_len, slots):
    tok_dev = tokens.shape[0]
    n_grp = lax.axis_size("grp")
    n_shard = lax.axis_size("shard")
    core = lax.axis_index("grp") % 2
    pairs = [(g, g ^ 1) for g in range(n_grp)]

    owner = prefix_owner[0]
    sliced = gather_by_a2a(prefix_kv[0], "grp", n_grp)
    chosen = lax.dynamic_index_in_dim(sliced, owner, 0, keepdims=False)
    prefix = gather_by_a2a(chosen, "shard", n_shard).reshape(-1, chosen.shape[-1])

    here = slots.reshape(tok_dev, 1) % tok_dev
    code = jnp.concatenate([here // 32, here % 32], axis=1).astype(tokens.dtype)
    code = jnp.pad(code, ((0, 0), (0, 126)))
    arrived = lax.all_to_all(jnp.concatenate([tokens, code], axis=1), "shard", 0, 0, tiled=True)
    d = tokens.shape[1]
    pos = arrived[:, d].astype(jnp.int32) * 32 + arrived[:, d + 1].astype(jnp.int32)
    onehot = (jnp.arange(tok_dev, dtype=jnp.int32)[:, None] == pos[None, :]).astype(jnp.bfloat16)
    placed = jnp.dot(onehot, arrived, preferred_element_type=jnp.float32).astype(jnp.bfloat16)[:, :d]
    normed = normalize(placed, gain)

    d = w_qkv.shape[0]
    kh = d // 2
    w_mine = lax.dynamic_slice_in_dim(w_qkv, core * kh, kh, axis=0)
    w_rows = lax.all_gather(w_mine, "shard", axis=1, tiled=True)
    w_other = lax.ppermute(w_rows, "grp", pairs)
    n_mine = lax.dynamic_slice_in_dim(normed, core * kh, kh, axis=1)
    n_other = lax.dynamic_slice_in_dim(normed, (1 - core) * kh, kh, axis=1)
    acc = jnp.dot(n_mine, w_rows, preferred_element_type=jnp.float32)
    acc = acc + jnp.dot(n_other, w_other, preferred_element_type=jnp.float32)
    qkv = acc.astype(jnp.bfloat16)

    lengths = suffix_len.reshape(-1)
    return attend(qkv, prefix, lengths[0])


def solution(mesh):
    return jax.shard_map(
        shards,
        mesh=mesh,
        in_specs=(
            P(("grp", "shard"), None),
            P(),
            P(None, "shard"),
            P("grp", "shard", None),
            P("grp"),
            P("grp", "shard"),
            P("grp", "shard"),
        ),
        out_specs=P(("grp", "shard"), None),
        check_vma=False,
    )
```

```python
import jax
import jax.numpy as jnp
from jax import lax
from jax.experimental import pallas as pl
from jax.experimental.pallas import tpu as pltpu
from jax.sharding import PartitionSpec as P


H = 10
HD = 256
WINDOW = 2048
TQ = 256


def normalize(rows, gain):
    rows32 = rows.astype(jnp.float32)
    factor = lax.rsqrt(jnp.mean(rows32 * rows32, axis=-1, keepdims=True) + 1e-06)
    return (rows32 * factor * gain).astype(jnp.bfloat16)


def _attn_kernel(len_ref, q_ref, pk_ref, pv_ref, sk_ref, sv_ref, o_ref, s_ref, p_ref):
    n = len_ref[0]
    pre = pk_ref.shape[0]
    count = q_ref.shape[0]
    nt = (((1,), (1,)), ((), ()))
    for i in range(count // TQ):
        r0 = i * TQ
        lp = pre - r0
        ns = r0 + TQ
        q = q_ref[r0:r0 + TQ, :] * jnp.asarray(HD ** (-0.5), q_ref.dtype)
        qpos = r0 + lax.broadcasted_iota(jnp.int32, (TQ, 1), 0)
        s_ref[:, :lp] = lax.dot_general(q, pk_ref[r0:, :], nt, preferred_element_type=jnp.float32)
        s_ref[:, lp:lp + ns] = lax.dot_general(q, sk_ref[:ns, :], nt, preferred_element_type=jnp.float32)
        ppos = r0 + lax.broadcasted_iota(jnp.int32, (1, TQ), 1)
        vis_p = (ppos > pre + qpos - WINDOW) & (ppos <= pre + qpos) & (ppos < pre + n)
        s_ref[:, :TQ] = jnp.where(vis_p, s_ref[:, :TQ], -1e30)
        spos = pre + lax.broadcasted_iota(jnp.int32, (1, ns), 1)
        vis_s = (spos > pre + qpos - WINDOW) & (spos <= pre + qpos) & (spos < pre + n)
        s_ref[:, lp:lp + ns] = jnp.where(vis_s, s_ref[:, lp:lp + ns], -1e30)
        s = s_ref[:, :lp + ns]
        top = jnp.max(s, axis=-1, keepdims=True)
        e = jnp.exp(s - top)
        s_ref[...] = e
        inv = 1.0 / jnp.sum(e, axis=-1, keepdims=True)
        p_ref[...] = (s_ref[...] * inv).astype(p_ref.dtype)
        acc = jnp.dot(p_ref[:, :lp], pv_ref[r0:, :], preferred_element_type=jnp.float32)
        out = acc + jnp.dot(p_ref[:, lp:lp + ns], sv_ref[:ns, :], preferred_element_type=jnp.float32)
        o_ref[r0:r0 + TQ, :] = jnp.where(qpos < n, out, 0.0).astype(o_ref.dtype)


def attend(qkv, prefix, length):
    count = qkv.shape[0]
    pre = prefix.shape[0]
    width = pre + TQ
    grid_spec = pltpu.PrefetchScalarGridSpec(
        num_scalar_prefetch=1,
        grid=(H,),
        in_specs=[
            pl.BlockSpec((count, HD), lambda h, n: (0, h)),
            pl.BlockSpec((pre, HD), lambda h, n: (0, 0)),
            pl.BlockSpec((pre, HD), lambda h, n: (0, 1)),
            pl.BlockSpec((count, HD), lambda h, n: (0, H)),
            pl.BlockSpec((count, HD), lambda h, n: (0, H + 1)),
        ],
        out_specs=pl.BlockSpec((count, HD), lambda h, n: (0, h)),
        scratch_shapes=[
            pltpu.VMEM((TQ, width), jnp.float32),
            pltpu.VMEM((TQ, width), jnp.bfloat16),
        ],
    )
    flops = 4 * H * count * width * HD
    return pl.pallas_call(
        _attn_kernel,
        out_shape=jax.ShapeDtypeStruct((count, H * HD), jnp.bfloat16),
        grid_spec=grid_spec,
        compiler_params=pltpu.CompilerParams(vmem_limit_bytes=48 * 1024 * 1024),
        cost_estimate=pl.CostEstimate(
            flops=flops,
            transcendentals=H * count * width,
            bytes_accessed=2 * (count * qkv.shape[1] + pre * prefix.shape[1] + count * H * HD),
        ),
    )(length.reshape(1).astype(jnp.int32), qkv, prefix, prefix, qkv, qkv)


def gather_by_a2a(piece, axis_name, count):
    spread = jnp.broadcast_to(piece[None], (count,) + piece.shape)
    return lax.all_to_all(spread, axis_name, 0, 0, tiled=True)


def ring_gather_plane(piece, axis_name):
    side = 4
    me = lax.axis_index(axis_name)
    z, x = me // side, me % side

    def shifted(d, along_x):
        pairs = []
        for zz in range(side):
            for xx in range(side):
                if along_x:
                    pairs.append((zz * side + xx, zz * side + (xx + d) % side))
                else:
                    pairs.append((zz * side + xx, ((zz + d) % side) * side + xx))
        return pairs

    def gather_line(block, along_x, at):
        left = lax.ppermute(block, axis_name, shifted(1, along_x))
        right = lax.ppermute(block, axis_name, shifted(-1, along_x))
        far = lax.ppermute(left, axis_name, shifted(1, along_x))
        line = jnp.zeros((side,) + block.shape, block.dtype)
        for d, b in ((0, block), (-1, left), (1, right), (2, far)):
            line = lax.dynamic_update_index_in_dim(line, b, (at + d) % side, 0)
        return line

    row = gather_line(piece, True, x)
    return gather_line(row, False, z)


def shards(tokens, gain, w_qkv, prefix_kv, prefix_owner, suffix_len, slots):
    tok_dev = tokens.shape[0]
    n_grp = lax.axis_size("grp")
    core = lax.axis_index("grp") % 2
    pairs = [(g, g ^ 1) for g in range(n_grp)]

    owner = prefix_owner[0]
    sliced = gather_by_a2a(prefix_kv[0], "grp", n_grp)
    chosen = lax.dynamic_index_in_dim(sliced, owner, 0, keepdims=False)
    prefix = ring_gather_plane(chosen, "shard").reshape(-1, chosen.shape[-1])

    here = slots.reshape(tok_dev, 1) % tok_dev
    code = jnp.concatenate([here // 32, here % 32], axis=1).astype(tokens.dtype)
    code = jnp.pad(code, ((0, 0), (0, 126)))
    arrived = lax.all_to_all(jnp.concatenate([tokens, code], axis=1), "shard", 0, 0, tiled=True)
    d = tokens.shape[1]
    pos = arrived[:, d].astype(jnp.int32) * 32 + arrived[:, d + 1].astype(jnp.int32)
    onehot = (jnp.arange(tok_dev, dtype=jnp.int32)[:, None] == pos[None, :]).astype(jnp.bfloat16)
    placed = jnp.dot(onehot, arrived, preferred_element_type=jnp.float32).astype(jnp.bfloat16)[:, :d]
    normed = normalize(placed, gain)

    d = w_qkv.shape[0]
    kh = d // 2
    w_mine = lax.dynamic_slice_in_dim(w_qkv, core * kh, kh, axis=0)
    w_rows = lax.all_gather(w_mine, "shard", axis=1, tiled=True)
    w_other = lax.ppermute(w_rows, "grp", pairs)
    n_mine = lax.dynamic_slice_in_dim(normed, core * kh, kh, axis=1)
    n_other = lax.dynamic_slice_in_dim(normed, (1 - core) * kh, kh, axis=1)
    acc = jnp.dot(n_mine, w_rows, preferred_element_type=jnp.float32)
    acc = acc + jnp.dot(n_other, w_other, preferred_element_type=jnp.float32)
    qkv = acc.astype(jnp.bfloat16)

    lengths = suffix_len.reshape(-1)
    return attend(qkv, prefix, lengths[0])


def solution(mesh):
    return jax.shard_map(
        shards,
        mesh=mesh,
        in_specs=(
            P(("grp", "shard"), None),
            P(),
            P(None, "shard"),
            P("grp", "shard", None),
            P("grp"),
            P("grp", "shard"),
            P("grp", "shard"),
        ),
        out_specs=P(("grp", "shard"), None),
        check_vma=False,
    )
```

```python
import jax
import jax.numpy as jnp
from jax import lax
from jax.experimental import pallas as pl
from jax.experimental.pallas import tpu as pltpu
from jax.sharding import PartitionSpec as P


H = 10
HD = 256
WINDOW = 2048
TQ = 256


def normalize(rows, gain):
    rows32 = rows.astype(jnp.float32)
    factor = lax.rsqrt(jnp.mean(rows32 * rows32, axis=-1, keepdims=True) + 1e-06)
    return (rows32 * factor * gain).astype(jnp.bfloat16)


def _attn_kernel(len_ref, q_ref, pk_ref, pv_ref, sk_ref, sv_ref, o_ref, s_ref, p_ref):
    n = len_ref[0]
    pre = pk_ref.shape[0]
    count = q_ref.shape[0]
    nt = (((1,), (1,)), ((), ()))
    for i in range(count // TQ):
        r0 = i * TQ
        lp = pre - r0
        ns = r0 + TQ
        q = q_ref[r0:r0 + TQ, :] * jnp.asarray(HD ** (-0.5), q_ref.dtype)
        qpos = r0 + lax.broadcasted_iota(jnp.int32, (TQ, 1), 0)
        s_ref[:, :lp] = lax.dot_general(q, pk_ref[r0:, :], nt, preferred_element_type=jnp.float32)
        s_ref[:, lp:lp + ns] = lax.dot_general(q, sk_ref[:ns, :], nt, preferred_element_type=jnp.float32)
        ppos = r0 + lax.broadcasted_iota(jnp.int32, (1, TQ), 1)
        vis_p = (ppos > pre + qpos - WINDOW) & (ppos <= pre + qpos) & (ppos < pre + n)
        s_ref[:, :TQ] = jnp.where(vis_p, s_ref[:, :TQ], -1e30)
        spos = pre + lax.broadcasted_iota(jnp.int32, (1, ns), 1)
        vis_s = (spos > pre + qpos - WINDOW) & (spos <= pre + qpos) & (spos < pre + n)
        s_ref[:, lp:lp + ns] = jnp.where(vis_s, s_ref[:, lp:lp + ns], -1e30)
        s = s_ref[:, :lp + ns]
        top = jnp.max(s, axis=-1, keepdims=True)
        e = jnp.exp(s - top)
        s_ref[...] = e
        inv = 1.0 / jnp.sum(e, axis=-1, keepdims=True)
        p_ref[...] = (s_ref[...] * inv).astype(p_ref.dtype)
        acc = jnp.dot(p_ref[:, :lp], pv_ref[r0:, :], preferred_element_type=jnp.float32)
        out = acc + jnp.dot(p_ref[:, lp:lp + ns], sv_ref[:ns, :], preferred_element_type=jnp.float32)
        o_ref[r0:r0 + TQ, :] = jnp.where(qpos < n, out, 0.0).astype(o_ref.dtype)


def attend(qkv, prefix, length):
    count = qkv.shape[0]
    pre = prefix.shape[0]
    width = pre + TQ
    grid_spec = pltpu.PrefetchScalarGridSpec(
        num_scalar_prefetch=1,
        grid=(H,),
        in_specs=[
            pl.BlockSpec((count, HD), lambda h, n: (0, h)),
            pl.BlockSpec((pre, HD), lambda h, n: (0, 0)),
            pl.BlockSpec((pre, HD), lambda h, n: (0, 1)),
            pl.BlockSpec((count, HD), lambda h, n: (0, H)),
            pl.BlockSpec((count, HD), lambda h, n: (0, H + 1)),
        ],
        out_specs=pl.BlockSpec((count, HD), lambda h, n: (0, h)),
        scratch_shapes=[
            pltpu.VMEM((TQ, width), jnp.float32),
            pltpu.VMEM((TQ, width), jnp.bfloat16),
        ],
    )
    flops = 4 * H * count * width * HD
    return pl.pallas_call(
        _attn_kernel,
        out_shape=jax.ShapeDtypeStruct((count, H * HD), jnp.bfloat16),
        grid_spec=grid_spec,
        compiler_params=pltpu.CompilerParams(vmem_limit_bytes=48 * 1024 * 1024),
        cost_estimate=pl.CostEstimate(
            flops=flops,
            transcendentals=H * count * width,
            bytes_accessed=2 * (count * qkv.shape[1] + pre * prefix.shape[1] + count * H * HD),
        ),
    )(length.reshape(1).astype(jnp.int32), qkv, prefix, prefix, qkv, qkv)


def gather_by_a2a(piece, axis_name, count):
    spread = jnp.broadcast_to(piece[None], (count,) + piece.shape)
    return lax.all_to_all(spread, axis_name, 0, 0, tiled=True)


def shards(tokens, gain, w_qkv, prefix_kv, prefix_owner, suffix_len, slots):
    tok_dev = tokens.shape[0]
    n_grp = lax.axis_size("grp")
    n_shard = lax.axis_size("shard")
    core = lax.axis_index("grp") % 2
    pairs = [(g, g ^ 1) for g in range(n_grp)]

    here = slots.reshape(tok_dev, 1) % tok_dev
    code = jnp.concatenate([here // 32, here % 32], axis=1).astype(tokens.dtype)
    code = jnp.pad(code, ((0, 0), (0, 126)))
    arrived = lax.all_to_all(jnp.concatenate([tokens, code], axis=1), "shard", 0, 0, tiled=True)
    local_prefix, arrived = lax.optimization_barrier((prefix_kv[0], arrived))
    owner = prefix_owner[0]
    sliced = gather_by_a2a(local_prefix, "grp", n_grp)
    chosen = lax.dynamic_index_in_dim(sliced, owner, 0, keepdims=False)
    prefix = gather_by_a2a(chosen, "shard", n_shard).reshape(-1, chosen.shape[-1])
    d = tokens.shape[1]
    pos = arrived[:, d].astype(jnp.int32) * 32 + arrived[:, d + 1].astype(jnp.int32)
    onehot = (jnp.arange(tok_dev, dtype=jnp.int32)[:, None] == pos[None, :]).astype(jnp.bfloat16)
    placed = jnp.dot(onehot, arrived, preferred_element_type=jnp.float32).astype(jnp.bfloat16)[:, :d]
    normed = normalize(placed, gain)

    d = w_qkv.shape[0]
    kh = d // 2
    kc = kh // 2
    acc = None
    for part in range(2):
        w_part = lax.dynamic_slice_in_dim(w_qkv, core * kh + part * kc, kc, axis=0)
        w_rows = lax.all_gather(w_part, "shard", axis=1, tiled=True)
        w_other = lax.ppermute(w_rows, "grp", pairs)
        n_mine = lax.dynamic_slice_in_dim(normed, core * kh + part * kc, kc, axis=1)
        n_other = lax.dynamic_slice_in_dim(normed, (1 - core) * kh + part * kc, kc, axis=1)
        term = jnp.dot(n_mine, w_rows, preferred_element_type=jnp.float32)
        term = term + jnp.dot(n_other, w_other, preferred_element_type=jnp.float32)
        acc = term if acc is None else acc + term
    qkv = acc.astype(jnp.bfloat16)

    lengths = suffix_len.reshape(-1)
    return attend(qkv, prefix, lengths[0])


def solution(mesh):
    return jax.shard_map(
        shards,
        mesh=mesh,
        in_specs=(
            P(("grp", "shard"), None),
            P(),
            P(None, "shard"),
            P("grp", "shard", None),
            P("grp"),
            P("grp", "shard"),
            P("grp", "shard"),
        ),
        out_specs=P(("grp", "shard"), None),
        check_vma=False,
    )
```

```python
import jax
import jax.numpy as jnp
from jax import lax
from jax.experimental import pallas as pl
from jax.experimental.pallas import tpu as pltpu
from jax.sharding import PartitionSpec as P


H = 10
HD = 256
WINDOW = 2048
TQ = 128


def normalize(rows, gain):
    rows32 = rows.astype(jnp.float32)
    factor = lax.rsqrt(jnp.mean(rows32 * rows32, axis=-1, keepdims=True) + 1e-06)
    return (rows32 * factor * gain).astype(jnp.bfloat16)


def _attn_kernel(len_ref, q_ref, pk_ref, pv_ref, sk_ref, sv_ref, o_ref, s_ref, p_ref):
    n = len_ref[0]
    pre = pk_ref.shape[1]
    count = q_ref.shape[0]
    for i in range(count // TQ):
        r0 = i * TQ
        lp = pre - r0
        ns = r0 + TQ
        q = q_ref[r0:r0 + TQ, :] * jnp.asarray(HD ** (-0.5), q_ref.dtype)
        qpos = r0 + lax.broadcasted_iota(jnp.int32, (TQ, 1), 0)
        s_ref[:, :lp] = jnp.dot(q, pk_ref[:, r0:], preferred_element_type=jnp.float32)
        s_ref[:, lp:lp + ns] = jnp.dot(q, sk_ref[:, :ns], preferred_element_type=jnp.float32)
        ppos = r0 + lax.broadcasted_iota(jnp.int32, (1, TQ), 1)
        vis_p = (ppos > pre + qpos - WINDOW) & (ppos <= pre + qpos) & (ppos < pre + n)
        s_ref[:, :TQ] = jnp.where(vis_p, s_ref[:, :TQ], -1e30)
        spos = pre + lax.broadcasted_iota(jnp.int32, (1, ns), 1)
        vis_s = (spos > pre + qpos - WINDOW) & (spos <= pre + qpos) & (spos < pre + n)
        s_ref[:, lp:lp + ns] = jnp.where(vis_s, s_ref[:, lp:lp + ns], -1e30)
        s = s_ref[:, :lp + ns]
        top = jnp.max(s, axis=-1, keepdims=True)
        e = jnp.exp(s - top)
        s_ref[...] = e
        inv = 1.0 / jnp.sum(e, axis=-1, keepdims=True)
        p_ref[...] = (s_ref[...] * inv).astype(p_ref.dtype)
        acc = jnp.dot(p_ref[:, :lp], pv_ref[r0:, :], preferred_element_type=jnp.float32)
        out = acc + jnp.dot(p_ref[:, lp:lp + ns], sv_ref[:ns, :], preferred_element_type=jnp.float32)
        o_ref[r0:r0 + TQ, :] = jnp.where(qpos < n, out, 0.0).astype(o_ref.dtype)


def attend(qkv, prefix, length):
    count = qkv.shape[0]
    pre = prefix.shape[0]
    width = pre + TQ
    keys_pre = prefix[:, :HD].T
    keys_suf = qkv[:, H * HD:(H + 1) * HD].T
    grid_spec = pltpu.PrefetchScalarGridSpec(
        num_scalar_prefetch=1,
        grid=(H,),
        in_specs=[
            pl.BlockSpec((count, HD), lambda h, n: (0, h)),
            pl.BlockSpec((HD, pre), lambda h, n: (0, 0)),
            pl.BlockSpec((pre, HD), lambda h, n: (0, 1)),
            pl.BlockSpec((HD, count), lambda h, n: (0, 0)),
            pl.BlockSpec((count, HD), lambda h, n: (0, H + 1)),
        ],
        out_specs=pl.BlockSpec((count, HD), lambda h, n: (0, h)),
        scratch_shapes=[
            pltpu.VMEM((TQ, width), jnp.float32),
            pltpu.VMEM((TQ, width), jnp.bfloat16),
        ],
    )
    flops = 4 * H * count * width * HD
    return pl.pallas_call(
        _attn_kernel,
        out_shape=jax.ShapeDtypeStruct((count, H * HD), jnp.bfloat16),
        grid_spec=grid_spec,
        compiler_params=pltpu.CompilerParams(vmem_limit_bytes=48 * 1024 * 1024),
        cost_estimate=pl.CostEstimate(
            flops=flops,
            transcendentals=H * count * width,
            bytes_accessed=2 * (count * qkv.shape[1] + pre * prefix.shape[1] + count * H * HD),
        ),
    )(length.reshape(1).astype(jnp.int32), qkv, keys_pre, prefix, keys_suf, qkv)


def gather_by_a2a(piece, axis_name, count):
    spread = jnp.broadcast_to(piece[None], (count,) + piece.shape)
    return lax.all_to_all(spread, axis_name, 0, 0, tiled=True)


def shards(tokens, gain, w_qkv, prefix_kv, prefix_owner, suffix_len, slots):
    tok_dev = tokens.shape[0]
    n_grp = lax.axis_size("grp")
    n_shard = lax.axis_size("shard")
    core = lax.axis_index("grp") % 2
    pairs = [(g, g ^ 1) for g in range(n_grp)]

    owner = prefix_owner[0]
    sliced = gather_by_a2a(prefix_kv[0], "grp", n_grp)
    chosen = lax.dynamic_index_in_dim(sliced, owner, 0, keepdims=False)
    prefix = gather_by_a2a(chosen, "shard", n_shard).reshape(-1, chosen.shape[-1])

    here = slots.reshape(tok_dev, 1) % tok_dev
    code = jnp.concatenate([here // 32, here % 32], axis=1).astype(tokens.dtype)
    code = jnp.pad(code, ((0, 0), (0, 126)))
    arrived = lax.all_to_all(jnp.concatenate([tokens, code], axis=1), "shard", 0, 0, tiled=True)
    d = tokens.shape[1]
    pos = arrived[:, d].astype(jnp.int32) * 32 + arrived[:, d + 1].astype(jnp.int32)
    onehot = (jnp.arange(tok_dev, dtype=jnp.int32)[:, None] == pos[None, :]).astype(jnp.bfloat16)
    placed = jnp.dot(onehot, arrived, preferred_element_type=jnp.float32).astype(jnp.bfloat16)[:, :d]
    normed = normalize(placed, gain)

    d = w_qkv.shape[0]
    kh = d // 2
    w_mine = lax.dynamic_slice_in_dim(w_qkv, core * kh, kh, axis=0)
    w_rows = lax.all_gather(w_mine, "shard", axis=1, tiled=True)
    n_mine = lax.dynamic_slice_in_dim(normed, core * kh, kh, axis=1)
    acc = jnp.dot(n_mine, w_rows, preferred_element_type=jnp.float32)
    kc = kh // 2
    for part in range(2):
        w_other = lax.ppermute(w_rows[part * kc:(part + 1) * kc], "grp", pairs)
        n_other = lax.dynamic_slice_in_dim(normed, (1 - core) * kh + part * kc, kc, axis=1)
        acc = acc + jnp.dot(n_other, w_other, preferred_element_type=jnp.float32)
    qkv = acc.astype(jnp.bfloat16)

    lengths = suffix_len.reshape(-1)
    return attend(qkv, prefix, lengths[0])


def solution(mesh):
    return jax.shard_map(
        shards,
        mesh=mesh,
        in_specs=(
            P(("grp", "shard"), None),
            P(),
            P(None, "shard"),
            P("grp", "shard", None),
            P("grp"),
            P("grp", "shard"),
            P("grp", "shard"),
        ),
        out_specs=P(("grp", "shard"), None),
        check_vma=False,
    )
```

```python
import jax
import jax.numpy as jnp
from jax import lax
from jax.experimental import pallas as pl
from jax.experimental.pallas import tpu as pltpu
from jax.sharding import PartitionSpec as P


H = 10
HD = 256
WINDOW = 2048
TQ = 256


def normalize(rows, gain):
    rows32 = rows.astype(jnp.float32)
    factor = lax.rsqrt(jnp.mean(rows32 * rows32, axis=-1, keepdims=True) + 1e-06)
    return (rows32 * factor * gain).astype(jnp.bfloat16)


def _attn_kernel(len_ref, q_ref, pk_ref, pv_ref, sk_ref, sv_ref, o_ref, s_ref, p_ref):
    n = len_ref[0]
    pre = pk_ref.shape[0]
    count = q_ref.shape[0]
    nt = (((1,), (1,)), ((), ()))
    for i in range(count // TQ):
        r0 = i * TQ
        lp = pre - r0
        ns = r0 + TQ
        q = q_ref[r0:r0 + TQ, :] * jnp.asarray(HD ** (-0.5), q_ref.dtype)
        qpos = r0 + lax.broadcasted_iota(jnp.int32, (TQ, 1), 0)
        s_ref[:, :lp] = lax.dot_general(q, pk_ref[r0:, :], nt, preferred_element_type=jnp.float32)
        s_ref[:, lp:lp + ns] = lax.dot_general(q, sk_ref[:ns, :], nt, preferred_element_type=jnp.float32)
        ppos = r0 + lax.broadcasted_iota(jnp.int32, (1, TQ), 1)
        vis_p = (ppos > pre + qpos - WINDOW) & (ppos <= pre + qpos) & (ppos < pre + n)
        s_ref[:, :TQ] = jnp.where(vis_p, s_ref[:, :TQ], -1e30)
        spos = pre + lax.broadcasted_iota(jnp.int32, (1, ns), 1)
        vis_s = (spos > pre + qpos - WINDOW) & (spos <= pre + qpos) & (spos < pre + n)
        s_ref[:, lp:lp + ns] = jnp.where(vis_s, s_ref[:, lp:lp + ns], -1e30)
        s = s_ref[:, :lp + ns]
        top = jnp.max(s, axis=-1, keepdims=True)
        e = jnp.exp(s - top)
        s_ref[...] = e
        inv = 1.0 / jnp.sum(e, axis=-1, keepdims=True)
        p_ref[...] = (s_ref[...] * inv).astype(p_ref.dtype)
        acc = jnp.dot(p_ref[:, :lp], pv_ref[r0:, :], preferred_element_type=jnp.float32)
        out = acc + jnp.dot(p_ref[:, lp:lp + ns], sv_ref[:ns, :], preferred_element_type=jnp.float32)
        o_ref[r0:r0 + TQ, :] = jnp.where(qpos < n, out, 0.0).astype(o_ref.dtype)


def attend(qkv, prefix, length):
    count = qkv.shape[0]
    pre = prefix.shape[0]
    width = pre + TQ
    grid_spec = pltpu.PrefetchScalarGridSpec(
        num_scalar_prefetch=1,
        grid=(H,),
        in_specs=[
            pl.BlockSpec((count, HD), lambda h, n: (0, h)),
            pl.BlockSpec((pre, HD), lambda h, n: (0, 0)),
            pl.BlockSpec((pre, HD), lambda h, n: (0, 1)),
            pl.BlockSpec((count, HD), lambda h, n: (0, H)),
            pl.BlockSpec((count, HD), lambda h, n: (0, H + 1)),
        ],
        out_specs=pl.BlockSpec((count, HD), lambda h, n: (0, h)),
        scratch_shapes=[
            pltpu.VMEM((TQ, width), jnp.float32),
            pltpu.VMEM((TQ, width), jnp.bfloat16),
        ],
    )
    flops = 4 * H * count * width * HD
    return pl.pallas_call(
        _attn_kernel,
        out_shape=jax.ShapeDtypeStruct((count, H * HD), jnp.bfloat16),
        grid_spec=grid_spec,
        compiler_params=pltpu.CompilerParams(vmem_limit_bytes=48 * 1024 * 1024),
        cost_estimate=pl.CostEstimate(
            flops=flops,
            transcendentals=H * count * width,
            bytes_accessed=2 * (count * qkv.shape[1] + pre * prefix.shape[1] + count * H * HD),
        ),
    )(length.reshape(1).astype(jnp.int32), qkv, prefix, prefix, qkv, qkv)


def gather_by_a2a(piece, axis_name, count):
    spread = jnp.broadcast_to(piece[None], (count,) + piece.shape)
    return lax.all_to_all(spread, axis_name, 0, 0, tiled=True)


def shards(tokens, gain, w_qkv, prefix_kv, prefix_owner, suffix_len, slots):
    tok_dev = tokens.shape[0]
    n_grp = lax.axis_size("grp")
    n_shard = lax.axis_size("shard")
    core = lax.axis_index("grp") % 2
    pairs = [(g, g ^ 1) for g in range(n_grp)]

    owner = prefix_owner[0]
    sliced = gather_by_a2a(prefix_kv[0], "grp", n_grp)
    chosen = lax.dynamic_index_in_dim(sliced, owner, 0, keepdims=False)
    prefix = gather_by_a2a(chosen, "shard", n_shard).reshape(-1, chosen.shape[-1])

    here = slots.reshape(tok_dev, 1) % tok_dev
    code = jnp.concatenate([here // 32, here % 32], axis=1).astype(tokens.dtype)
    code = jnp.pad(code, ((0, 0), (0, 126)))
    arrived = lax.all_to_all(jnp.concatenate([tokens, code], axis=1), "shard", 0, 0, tiled=True)
    d = tokens.shape[1]
    pos = arrived[:, d].astype(jnp.int32) * 32 + arrived[:, d + 1].astype(jnp.int32)
    onehot = (jnp.arange(tok_dev, dtype=jnp.int32)[:, None] == pos[None, :]).astype(jnp.bfloat16)
    placed = jnp.dot(onehot, arrived, preferred_element_type=jnp.float32).astype(jnp.bfloat16)[:, :d]
    normed = normalize(placed, gain)

    d = w_qkv.shape[0]
    nb = n_grp
    kb = d // nb
    g = lax.axis_index("grp")
    w_piece = lax.dynamic_slice_in_dim(w_qkv, g * kb, kb, axis=0)
    w_block = lax.all_gather(w_piece, "shard", axis=1, tiled=True)
    same_core = [list(range(c, n_grp, 2)) for c in range(2)]
    w_rows = lax.all_gather(w_block, "grp", axis=0, tiled=True, axis_index_groups=same_core)
    w_other = lax.ppermute(w_rows, "grp", pairs)
    blocks = normed.reshape(tok_dev, nb // 2, 2, kb)
    n_even = blocks[:, :, 0, :].reshape(tok_dev, d // 2)
    n_odd = blocks[:, :, 1, :].reshape(tok_dev, d // 2)
    is0 = core == 0
    n_mine = jnp.where(is0, n_even, n_odd)
    n_other = jnp.where(is0, n_odd, n_even)
    acc = jnp.dot(n_mine, w_rows, preferred_element_type=jnp.float32)
    acc = acc + jnp.dot(n_other, w_other, preferred_element_type=jnp.float32)
    qkv = acc.astype(jnp.bfloat16)

    lengths = suffix_len.reshape(-1)
    return attend(qkv, prefix, lengths[0])


def solution(mesh):
    return jax.shard_map(
        shards,
        mesh=mesh,
        in_specs=(
            P(("grp", "shard"), None),
            P(),
            P(None, "shard"),
            P("grp", "shard", None),
            P("grp"),
            P("grp", "shard"),
            P("grp", "shard"),
        ),
        out_specs=P(("grp", "shard"), None),
        check_vma=False,
    )
```

```python
import jax
import jax.numpy as jnp
from jax import lax
from jax.experimental import pallas as pl
from jax.experimental.pallas import tpu as pltpu
from jax.sharding import PartitionSpec as P


H = 10
HD = 256
WINDOW = 2048
TQ = 256


def normalize(rows, gain):
    rows32 = rows.astype(jnp.float32)
    factor = lax.rsqrt(jnp.mean(rows32 * rows32, axis=-1, keepdims=True) + 1e-06)
    return (rows32 * factor * gain).astype(jnp.bfloat16)


def _attn_kernel(len_ref, q_ref, pk_ref, pv_ref, sk_ref, sv_ref, o_ref, s_ref, p_ref):
    n = len_ref[0]
    pre = pk_ref.shape[0]
    count = q_ref.shape[0]
    nt = (((1,), (1,)), ((), ()))
    for i in range(count // TQ):
        r0 = i * TQ
        lp = pre - r0
        ns = r0 + TQ
        q = q_ref[r0:r0 + TQ, :] * jnp.asarray(HD ** (-0.5), q_ref.dtype)
        qpos = r0 + lax.broadcasted_iota(jnp.int32, (TQ, 1), 0)
        s_ref[:, :lp] = lax.dot_general(q, pk_ref[r0:, :], nt, preferred_element_type=jnp.float32)
        s_ref[:, lp:lp + ns] = lax.dot_general(q, sk_ref[:ns, :], nt, preferred_element_type=jnp.float32)
        ppos = r0 + lax.broadcasted_iota(jnp.int32, (1, TQ), 1)
        vis_p = (ppos > pre + qpos - WINDOW) & (ppos <= pre + qpos) & (ppos < pre + n)
        s_ref[:, :TQ] = jnp.where(vis_p, s_ref[:, :TQ], -1e30)
        spos = pre + lax.broadcasted_iota(jnp.int32, (1, ns), 1)
        vis_s = (spos > pre + qpos - WINDOW) & (spos <= pre + qpos) & (spos < pre + n)
        s_ref[:, lp:lp + ns] = jnp.where(vis_s, s_ref[:, lp:lp + ns], -1e30)
        s = s_ref[:, :lp + ns]
        top = jnp.max(s, axis=-1, keepdims=True)
        e = jnp.exp(s - top)
        s_ref[...] = e
        inv = 1.0 / jnp.sum(e, axis=-1, keepdims=True)
        p_ref[...] = (s_ref[...] * inv).astype(p_ref.dtype)
        acc = jnp.dot(p_ref[:, :lp], pv_ref[r0:, :], preferred_element_type=jnp.float32)
        out = acc + jnp.dot(p_ref[:, lp:lp + ns], sv_ref[:ns, :], preferred_element_type=jnp.float32)
        o_ref[r0:r0 + TQ, :] = jnp.where(qpos < n, out, 0.0).astype(o_ref.dtype)


def attend(qkv, prefix, length):
    count = qkv.shape[0]
    pre = prefix.shape[0]
    width = pre + TQ
    grid_spec = pltpu.PrefetchScalarGridSpec(
        num_scalar_prefetch=1,
        grid=(H,),
        in_specs=[
            pl.BlockSpec((count, HD), lambda h, n: (0, h)),
            pl.BlockSpec((pre, HD), lambda h, n: (0, 0)),
            pl.BlockSpec((pre, HD), lambda h, n: (0, 1)),
            pl.BlockSpec((count, HD), lambda h, n: (0, H)),
            pl.BlockSpec((count, HD), lambda h, n: (0, H + 1)),
        ],
        out_specs=pl.BlockSpec((count, HD), lambda h, n: (0, h)),
        scratch_shapes=[
            pltpu.VMEM((TQ, width), jnp.float32),
            pltpu.VMEM((TQ, width), jnp.bfloat16),
        ],
    )
    flops = 4 * H * count * width * HD
    return pl.pallas_call(
        _attn_kernel,
        out_shape=jax.ShapeDtypeStruct((count, H * HD), jnp.bfloat16),
        grid_spec=grid_spec,
        compiler_params=pltpu.CompilerParams(vmem_limit_bytes=48 * 1024 * 1024),
        cost_estimate=pl.CostEstimate(
            flops=flops,
            transcendentals=H * count * width,
            bytes_accessed=2 * (count * qkv.shape[1] + pre * prefix.shape[1] + count * H * HD),
        ),
    )(length.reshape(1).astype(jnp.int32), qkv, prefix, prefix, qkv, qkv)


def gather_by_a2a(piece, axis_name, count):
    spread = jnp.broadcast_to(piece[None], (count,) + piece.shape)
    return lax.all_to_all(spread, axis_name, 0, 0, tiled=True)


def shards(tokens, gain, w_qkv, prefix_kv, prefix_owner, suffix_len, slots):
    tok_dev = tokens.shape[0]
    n_grp = lax.axis_size("grp")
    n_shard = lax.axis_size("shard")
    core = lax.axis_index("grp") % 2
    pairs = [(g, g ^ 1) for g in range(n_grp)]

    sliced = lax.all_gather(prefix_kv[0], "grp", axis=0)
    owner = prefix_owner[0]
    chosen = lax.dynamic_index_in_dim(sliced, owner, 0, keepdims=False)
    prefix = gather_by_a2a(chosen, "shard", n_shard).reshape(-1, chosen.shape[-1])

    here = slots.reshape(tok_dev, 1) % tok_dev
    code = jnp.concatenate([here // 32, here % 32], axis=1).astype(tokens.dtype)
    code = jnp.pad(code, ((0, 0), (0, 126)))
    arrived = lax.all_to_all(jnp.concatenate([tokens, code], axis=1), "shard", 0, 0, tiled=True)
    d = tokens.shape[1]
    pos = arrived[:, d].astype(jnp.int32) * 32 + arrived[:, d + 1].astype(jnp.int32)
    onehot = (jnp.arange(tok_dev, dtype=jnp.int32)[:, None] == pos[None, :]).astype(jnp.bfloat16)
    placed = jnp.dot(onehot, arrived, preferred_element_type=jnp.float32).astype(jnp.bfloat16)[:, :d]
    normed = normalize(placed, gain)

    d = w_qkv.shape[0]
    kh = d // 2
    w_mine = lax.dynamic_slice_in_dim(w_qkv, core * kh, kh, axis=0)
    w_rows = lax.all_gather(w_mine, "shard", axis=1, tiled=True)
    w_other = lax.ppermute(w_rows, "grp", pairs)
    n_mine = lax.dynamic_slice_in_dim(normed, core * kh, kh, axis=1)
    n_other = lax.dynamic_slice_in_dim(normed, (1 - core) * kh, kh, axis=1)
    acc = jnp.dot(n_mine, w_rows, preferred_element_type=jnp.float32)
    acc = acc + jnp.dot(n_other, w_other, preferred_element_type=jnp.float32)
    qkv = acc.astype(jnp.bfloat16)

    lengths = suffix_len.reshape(-1)
    return attend(qkv, prefix, lengths[0])


def solution(mesh):
    return jax.shard_map(
        shards,
        mesh=mesh,
        in_specs=(
            P(("grp", "shard"), None),
            P(),
            P(None, "shard"),
            P("grp", "shard", None),
            P("grp"),
            P("grp", "shard"),
            P("grp", "shard"),
        ),
        out_specs=P(("grp", "shard"), None),
        check_vma=False,
    )
```

```python
import jax
import jax.numpy as jnp
from jax import lax
from jax.experimental import pallas as pl
from jax.experimental.pallas import tpu as pltpu
from jax.sharding import PartitionSpec as P


H = 10
HD = 256
WINDOW = 2048
TQ = 256


def normalize(rows, gain):
    rows32 = rows.astype(jnp.float32)
    factor = lax.rsqrt(jnp.mean(rows32 * rows32, axis=-1, keepdims=True) + 1e-06)
    return (rows32 * factor * gain).astype(jnp.bfloat16)


def _attn_kernel(len_ref, q_ref, pk_ref, pv_ref, sk_ref, sv_ref, o_ref, s_ref, p_ref):
    n = len_ref[0]
    pre = pk_ref.shape[0]
    count = q_ref.shape[0]
    nt = (((1,), (1,)), ((), ()))
    for i in range(count // TQ):
        r0 = i * TQ
        lp = pre - r0
        ns = r0 + TQ
        q = q_ref[r0:r0 + TQ, :] * jnp.asarray(HD ** (-0.5), q_ref.dtype)
        qpos = r0 + lax.broadcasted_iota(jnp.int32, (TQ, 1), 0)
        s_ref[:, :lp] = lax.dot_general(q, pk_ref[r0:, :], nt, preferred_element_type=jnp.float32)
        s_ref[:, lp:lp + ns] = lax.dot_general(q, sk_ref[:ns, :], nt, preferred_element_type=jnp.float32)
        ppos = r0 + lax.broadcasted_iota(jnp.int32, (1, TQ), 1)
        vis_p = (ppos > pre + qpos - WINDOW) & (ppos <= pre + qpos) & (ppos < pre + n)
        s_ref[:, :TQ] = jnp.where(vis_p, s_ref[:, :TQ], -1e30)
        spos = pre + lax.broadcasted_iota(jnp.int32, (1, ns), 1)
        vis_s = (spos > pre + qpos - WINDOW) & (spos <= pre + qpos) & (spos < pre + n)
        s_ref[:, lp:lp + ns] = jnp.where(vis_s, s_ref[:, lp:lp + ns], -1e30)
        s = s_ref[:, :lp + ns]
        top = jnp.max(s, axis=-1, keepdims=True)
        e = jnp.exp(s - top)
        s_ref[...] = e
        inv = 1.0 / jnp.sum(e, axis=-1, keepdims=True)
        p_ref[...] = (s_ref[...] * inv).astype(p_ref.dtype)
        acc = jnp.dot(p_ref[:, :lp], pv_ref[r0:, :], preferred_element_type=jnp.float32)
        out = acc + jnp.dot(p_ref[:, lp:lp + ns], sv_ref[:ns, :], preferred_element_type=jnp.float32)
        o_ref[r0:r0 + TQ, :] = jnp.where(qpos < n, out, 0.0).astype(o_ref.dtype)


def attend(qkv, prefix, length):
    count = qkv.shape[0]
    pre = prefix.shape[0]
    width = pre + TQ
    grid_spec = pltpu.PrefetchScalarGridSpec(
        num_scalar_prefetch=1,
        grid=(H,),
        in_specs=[
            pl.BlockSpec((count, HD), lambda h, n: (0, h)),
            pl.BlockSpec((pre, HD), lambda h, n: (0, 0)),
            pl.BlockSpec((pre, HD), lambda h, n: (0, 1)),
            pl.BlockSpec((count, HD), lambda h, n: (0, H)),
            pl.BlockSpec((count, HD), lambda h, n: (0, H + 1)),
        ],
        out_specs=pl.BlockSpec((count, HD), lambda h, n: (0, h)),
        scratch_shapes=[
            pltpu.VMEM((TQ, width), jnp.float32),
            pltpu.VMEM((TQ, width), jnp.bfloat16),
        ],
    )
    flops = 4 * H * count * width * HD
    return pl.pallas_call(
        _attn_kernel,
        out_shape=jax.ShapeDtypeStruct((count, H * HD), jnp.bfloat16),
        grid_spec=grid_spec,
        compiler_params=pltpu.CompilerParams(vmem_limit_bytes=48 * 1024 * 1024),
        cost_estimate=pl.CostEstimate(
            flops=flops,
            transcendentals=H * count * width,
            bytes_accessed=2 * (count * qkv.shape[1] + pre * prefix.shape[1] + count * H * HD),
        ),
    )(length.reshape(1).astype(jnp.int32), qkv, prefix, prefix, qkv, qkv)


def gather_by_a2a(piece, axis_name, count):
    spread = jnp.broadcast_to(piece[None], (count,) + piece.shape)
    return lax.all_to_all(spread, axis_name, 0, 0, tiled=True)


def shards(tokens, gain, w_qkv, prefix_kv, prefix_owner, suffix_len, slots):
    tok_dev = tokens.shape[0]
    n_grp = lax.axis_size("grp")
    n_shard = lax.axis_size("shard")

    owner = prefix_owner[0]
    sliced = gather_by_a2a(prefix_kv[0], "grp", n_grp)
    chosen = lax.dynamic_index_in_dim(sliced, owner, 0, keepdims=False)
    prefix = gather_by_a2a(chosen, "shard", n_shard).reshape(-1, chosen.shape[-1])

    here = slots.reshape(tok_dev, 1) % tok_dev
    code = jnp.concatenate([here // 32, here % 32], axis=1).astype(tokens.dtype)
    code = jnp.pad(code, ((0, 0), (0, 126)))
    arrived = lax.all_to_all(jnp.concatenate([tokens, code], axis=1), "shard", 0, 0, tiled=True)
    d = tokens.shape[1]
    pos = arrived[:, d].astype(jnp.int32) * 32 + arrived[:, d + 1].astype(jnp.int32)
    onehot = (jnp.arange(tok_dev, dtype=jnp.int32)[:, None] == pos[None, :]).astype(jnp.bfloat16)
    placed = jnp.dot(onehot, arrived, preferred_element_type=jnp.float32).astype(jnp.bfloat16)[:, :d]
    normed = normalize(placed, gain)

    d = w_qkv.shape[0]
    kb = d // n_grp
    g = lax.axis_index("grp")
    w_piece = lax.dynamic_slice_in_dim(w_qkv, g * kb, kb, axis=0)
    pieces = lax.all_gather(w_piece, ("grp", "shard"), axis=0)
    pieces = pieces.reshape(n_grp, n_shard, kb, w_qkv.shape[1])
    acc = jnp.einsum("ngr,gsrc->nsc", normed.reshape(tok_dev, n_grp, kb), pieces,
                     preferred_element_type=jnp.float32).reshape(tok_dev, -1)
    qkv = acc.astype(jnp.bfloat16)

    lengths = suffix_len.reshape(-1)
    return attend(qkv, prefix, lengths[0])


def solution(mesh):
    return jax.shard_map(
        shards,
        mesh=mesh,
        in_specs=(
            P(("grp", "shard"), None),
            P(),
            P(None, "shard"),
            P("grp", "shard", None),
            P("grp"),
            P("grp", "shard"),
            P("grp", "shard"),
        ),
        out_specs=P(("grp", "shard"), None),
        check_vma=False,
    )
```

```python
import jax
import jax.numpy as jnp
from jax import lax
from jax.experimental import pallas as pl
from jax.experimental.pallas import tpu as pltpu
from jax.sharding import PartitionSpec as P


H = 10
HD = 256
WINDOW = 2048
TQ = 256
HPAIR = 5


def normalize(rows, gain):
    rows32 = rows.astype(jnp.float32)
    factor = lax.rsqrt(jnp.mean(rows32 * rows32, axis=-1, keepdims=True) + 1e-06)
    return (rows32 * factor * gain).astype(jnp.bfloat16)


def _attn_kernel(len_ref, q_ref, pk_ref, pv_ref, sk_ref, sv_ref, o_ref, s_ref, p_ref):
    n = len_ref[0]
    pre = pk_ref.shape[0]
    count = q_ref.shape[0]
    nt = (((1,), (1,)), ((), ()))
    for hh in range(q_ref.shape[1] // HD):
        for i in range(count // TQ):
            r0 = i * TQ
            c0 = hh * HD
            lp = pre - r0
            ns = r0 + TQ
            q = q_ref[r0:r0 + TQ, c0:c0 + HD] * jnp.asarray(HD ** (-0.5), q_ref.dtype)
            qpos = r0 + lax.broadcasted_iota(jnp.int32, (TQ, 1), 0)
            s_ref[:, :lp] = lax.dot_general(q, pk_ref[r0:, :], nt, preferred_element_type=jnp.float32)
            s_ref[:, lp:lp + ns] = lax.dot_general(q, sk_ref[:ns, :], nt, preferred_element_type=jnp.float32)
            ppos = r0 + lax.broadcasted_iota(jnp.int32, (1, TQ), 1)
            vis_p = (ppos > pre + qpos - WINDOW) & (ppos <= pre + qpos) & (ppos < pre + n)
            s_ref[:, :TQ] = jnp.where(vis_p, s_ref[:, :TQ], -1e30)
            spos = pre + lax.broadcasted_iota(jnp.int32, (1, ns), 1)
            vis_s = (spos > pre + qpos - WINDOW) & (spos <= pre + qpos) & (spos < pre + n)
            s_ref[:, lp:lp + ns] = jnp.where(vis_s, s_ref[:, lp:lp + ns], -1e30)
            s = s_ref[:, :lp + ns]
            top = jnp.max(s, axis=-1, keepdims=True)
            e = jnp.exp(s - top)
            s_ref[...] = e
            inv = 1.0 / jnp.sum(e, axis=-1, keepdims=True)
            p_ref[...] = (s_ref[...] * inv).astype(p_ref.dtype)
            acc = jnp.dot(p_ref[:, :lp], pv_ref[r0:, :], preferred_element_type=jnp.float32)
            out = acc + jnp.dot(p_ref[:, lp:lp + ns], sv_ref[:ns, :], preferred_element_type=jnp.float32)
            o_ref[r0:r0 + TQ, c0:c0 + HD] = jnp.where(qpos < n, out, 0.0).astype(o_ref.dtype)


def attend(qkv, prefix, length):
    count = qkv.shape[0]
    pre = prefix.shape[0]
    width = pre + TQ
    grid_spec = pltpu.PrefetchScalarGridSpec(
        num_scalar_prefetch=1,
        grid=(H // HPAIR,),
        in_specs=[
            pl.BlockSpec((count, HPAIR * HD), lambda h, n: (0, h)),
            pl.BlockSpec((pre, HD), lambda h, n: (0, 0)),
            pl.BlockSpec((pre, HD), lambda h, n: (0, 1)),
            pl.BlockSpec((count, HD), lambda h, n: (0, H)),
            pl.BlockSpec((count, HD), lambda h, n: (0, H + 1)),
        ],
        out_specs=pl.BlockSpec((count, HPAIR * HD), lambda h, n: (0, h)),
        scratch_shapes=[
            pltpu.VMEM((TQ, width), jnp.float32),
            pltpu.VMEM((TQ, width), jnp.bfloat16),
        ],
    )
    flops = 4 * H * count * width * HD
    return pl.pallas_call(
        _attn_kernel,
        out_shape=jax.ShapeDtypeStruct((count, H * HD), jnp.bfloat16),
        grid_spec=grid_spec,
        compiler_params=pltpu.CompilerParams(vmem_limit_bytes=48 * 1024 * 1024),
        cost_estimate=pl.CostEstimate(
            flops=flops,
            transcendentals=H * count * width,
            bytes_accessed=2 * (count * qkv.shape[1] + pre * prefix.shape[1] + count * H * HD),
        ),
    )(length.reshape(1).astype(jnp.int32), qkv, prefix, prefix, qkv, qkv)


def gather_by_a2a(piece, axis_name, count):
    spread = jnp.broadcast_to(piece[None], (count,) + piece.shape)
    return lax.all_to_all(spread, axis_name, 0, 0, tiled=True)


def shards(tokens, gain, w_qkv, prefix_kv, prefix_owner, suffix_len, slots):
    tok_dev = tokens.shape[0]
    n_grp = lax.axis_size("grp")
    n_shard = lax.axis_size("shard")
    core = lax.axis_index("grp") % 2
    pairs = [(g, g ^ 1) for g in range(n_grp)]

    owner = prefix_owner[0]
    sliced = gather_by_a2a(prefix_kv[0], "grp", n_grp)
    chosen = lax.dynamic_index_in_dim(sliced, owner, 0, keepdims=False)
    prefix = gather_by_a2a(chosen, "shard", n_shard).reshape(-1, chosen.shape[-1])

    here = slots.reshape(tok_dev, 1) % tok_dev
    code = jnp.concatenate([here // 32, here % 32], axis=1).astype(tokens.dtype)
    code = jnp.pad(code, ((0, 0), (0, 126)))
    sent = jnp.concatenate([tokens, code], axis=1)
    prefix, sent = lax.optimization_barrier((prefix, sent))
    arrived = lax.all_to_all(sent, "shard", 0, 0, tiled=True)
    d = tokens.shape[1]
    pos = arrived[:, d].astype(jnp.int32) * 32 + arrived[:, d + 1].astype(jnp.int32)
    onehot = (jnp.arange(tok_dev, dtype=jnp.int32)[:, None] == pos[None, :]).astype(jnp.bfloat16)
    placed = jnp.dot(onehot, arrived, preferred_element_type=jnp.float32).astype(jnp.bfloat16)[:, :d]
    normed = normalize(placed, gain)

    d = w_qkv.shape[0]
    kh = d // 2
    w_mine = lax.dynamic_slice_in_dim(w_qkv, core * kh, kh, axis=0)
    w_rows = lax.all_gather(w_mine, "shard", axis=1, tiled=True)
    w_other = lax.ppermute(w_rows, "grp", pairs)
    n_mine = lax.dynamic_slice_in_dim(normed, core * kh, kh, axis=1)
    n_other = lax.dynamic_slice_in_dim(normed, (1 - core) * kh, kh, axis=1)
    acc = jnp.dot(n_mine, w_rows, preferred_element_type=jnp.float32)
    acc = acc + jnp.dot(n_other, w_other, preferred_element_type=jnp.float32)
    qkv = acc.astype(jnp.bfloat16)

    lengths = suffix_len.reshape(-1)
    return attend(qkv, prefix, lengths[0])


def solution(mesh):
    return jax.shard_map(
        shards,
        mesh=mesh,
        in_specs=(
            P(("grp", "shard"), None),
            P(),
            P(None, "shard"),
            P("grp", "shard", None),
            P("grp"),
            P("grp", "shard"),
            P("grp", "shard"),
        ),
        out_specs=P(("grp", "shard"), None),
        check_vma=False,
    )
```

```python
import jax
import jax.numpy as jnp
from jax import lax
from jax.experimental import pallas as pl
from jax.experimental.pallas import tpu as pltpu
from jax.sharding import PartitionSpec as P


H = 10
HD = 256
WINDOW = 2048
TQ = 256
HPAIR = 10


def normalize(rows, gain):
    rows32 = rows.astype(jnp.float32)
    factor = lax.rsqrt(jnp.mean(rows32 * rows32, axis=-1, keepdims=True) + 1e-06)
    return (rows32 * factor * gain).astype(jnp.bfloat16)


def _attn_kernel(len_ref, q_ref, pk_ref, pv_ref, sk_ref, sv_ref, o_ref, s_ref, p_ref):
    n = len_ref[0]
    pre = pk_ref.shape[0]
    count = q_ref.shape[0]
    nt = (((1,), (1,)), ((), ()))
    for hh in range(q_ref.shape[1] // HD):
        for i in range(count // TQ):
            r0 = i * TQ
            c0 = hh * HD
            lp = pre - r0
            ns = r0 + TQ
            q = q_ref[r0:r0 + TQ, c0:c0 + HD] * jnp.asarray(HD ** (-0.5), q_ref.dtype)
            qpos = r0 + lax.broadcasted_iota(jnp.int32, (TQ, 1), 0)
            s_ref[:, :lp] = lax.dot_general(q, pk_ref[r0:, :], nt, preferred_element_type=jnp.float32)
            s_ref[:, lp:lp + ns] = lax.dot_general(q, sk_ref[:ns, :], nt, preferred_element_type=jnp.float32)
            ppos = r0 + lax.broadcasted_iota(jnp.int32, (1, TQ), 1)
            vis_p = (ppos > pre + qpos - WINDOW) & (ppos <= pre + qpos) & (ppos < pre + n)
            s_ref[:, :TQ] = jnp.where(vis_p, s_ref[:, :TQ], -1e30)
            spos = pre + lax.broadcasted_iota(jnp.int32, (1, ns), 1)
            vis_s = (spos > pre + qpos - WINDOW) & (spos <= pre + qpos) & (spos < pre + n)
            s_ref[:, lp:lp + ns] = jnp.where(vis_s, s_ref[:, lp:lp + ns], -1e30)
            s = s_ref[:, :lp + ns]
            top = jnp.max(s, axis=-1, keepdims=True)
            e = jnp.exp(s - top)
            inv = 1.0 / jnp.sum(e, axis=-1, keepdims=True)
            p_ref[...] = (e * inv).astype(p_ref.dtype)
            acc = jnp.dot(p_ref[:, :lp], pv_ref[r0:, :], preferred_element_type=jnp.float32)
            out = acc + jnp.dot(p_ref[:, lp:lp + ns], sv_ref[:ns, :], preferred_element_type=jnp.float32)
            o_ref[r0:r0 + TQ, c0:c0 + HD] = jnp.where(qpos < n, out, 0.0).astype(o_ref.dtype)


def attend(qkv, prefix, length):
    count = qkv.shape[0]
    pre = prefix.shape[0]
    width = pre + TQ
    grid_spec = pltpu.PrefetchScalarGridSpec(
        num_scalar_prefetch=1,
        grid=(H // HPAIR,),
        in_specs=[
            pl.BlockSpec((count, HPAIR * HD), lambda h, n: (0, h)),
            pl.BlockSpec((pre, HD), lambda h, n: (0, 0)),
            pl.BlockSpec((pre, HD), lambda h, n: (0, 1)),
            pl.BlockSpec((count, HD), lambda h, n: (0, H)),
            pl.BlockSpec((count, HD), lambda h, n: (0, H + 1)),
        ],
        out_specs=pl.BlockSpec((count, HPAIR * HD), lambda h, n: (0, h)),
        scratch_shapes=[
            pltpu.VMEM((TQ, width), jnp.float32),
            pltpu.VMEM((TQ, width), jnp.bfloat16),
        ],
    )
    flops = 4 * H * count * width * HD
    return pl.pallas_call(
        _attn_kernel,
        out_shape=jax.ShapeDtypeStruct((count, H * HD), jnp.bfloat16),
        grid_spec=grid_spec,
        compiler_params=pltpu.CompilerParams(vmem_limit_bytes=48 * 1024 * 1024),
        cost_estimate=pl.CostEstimate(
            flops=flops,
            transcendentals=H * count * width,
            bytes_accessed=2 * (count * qkv.shape[1] + pre * prefix.shape[1] + count * H * HD),
        ),
    )(length.reshape(1).astype(jnp.int32), qkv, prefix, prefix, qkv, qkv)


def gather_by_a2a(piece, axis_name, count):
    spread = jnp.broadcast_to(piece[None], (count,) + piece.shape)
    return lax.all_to_all(spread, axis_name, 0, 0, tiled=True)


def shards(tokens, gain, w_qkv, prefix_kv, prefix_owner, suffix_len, slots):
    tok_dev = tokens.shape[0]
    n_grp = lax.axis_size("grp")
    n_shard = lax.axis_size("shard")
    core = lax.axis_index("grp") % 2
    pairs = [(g, g ^ 1) for g in range(n_grp)]

    owner = prefix_owner[0]
    sliced = gather_by_a2a(prefix_kv[0], "grp", n_grp)
    chosen = lax.dynamic_index_in_dim(sliced, owner, 0, keepdims=False)
    prefix = gather_by_a2a(chosen, "shard", n_shard).reshape(-1, chosen.shape[-1])

    here = slots.reshape(tok_dev, 1) % tok_dev
    code = jnp.concatenate([here // 32, here % 32], axis=1).astype(tokens.dtype)
    code = jnp.pad(code, ((0, 0), (0, 126)))
    arrived = lax.all_to_all(jnp.concatenate([tokens, code], axis=1), "shard", 0, 0, tiled=True)
    d = tokens.shape[1]
    pos = arrived[:, d].astype(jnp.int32) * 32 + arrived[:, d + 1].astype(jnp.int32)
    onehot = (jnp.arange(tok_dev, dtype=jnp.int32)[:, None] == pos[None, :]).astype(jnp.bfloat16)
    placed = jnp.dot(onehot, arrived, preferred_element_type=jnp.float32).astype(jnp.bfloat16)[:, :d]
    normed = normalize(placed, gain)

    d = w_qkv.shape[0]
    kh = d // 2
    w_mine = lax.dynamic_slice_in_dim(w_qkv, core * kh, kh, axis=0)
    w_rows = lax.all_gather(w_mine, "shard", axis=1, tiled=True)
    w_other = lax.ppermute(w_rows, "grp", pairs)
    n_mine = lax.dynamic_slice_in_dim(normed, core * kh, kh, axis=1)
    n_other = lax.dynamic_slice_in_dim(normed, (1 - core) * kh, kh, axis=1)
    acc = jnp.dot(n_mine, w_rows, preferred_element_type=jnp.float32)
    acc = acc + jnp.dot(n_other, w_other, preferred_element_type=jnp.float32)
    qkv = acc.astype(jnp.bfloat16)

    lengths = suffix_len.reshape(-1)
    return attend(qkv, prefix, lengths[0])


def solution(mesh):
    return jax.shard_map(
        shards,
        mesh=mesh,
        in_specs=(
            P(("grp", "shard"), None),
            P(),
            P(None, "shard"),
            P("grp", "shard", None),
            P("grp"),
            P("grp", "shard"),
            P("grp", "shard"),
        ),
        out_specs=P(("grp", "shard"), None),
        check_vma=False,
    )
```
